256 devices in a mesh: row: 64 (over z, y, core), col: 4 (over x).
Axes of the slice: x: 4, y: 4, z: 8, core: 2. Of those that a mesh axis runs over, the one named last changes fastest.
Arguments:
- panel_adj: float32 [24576, 512], P('row', 'col'), may hold values from -16 to 16
- inv_tile: float32 [512, 512], P('col'), may hold values from -1 to 2, as said below
- factor_panel: float32 [24576, 512], P('row', 'col'), may hold values from -0.0390625 to 0.0390625
- block_row: float32 [512, 8192], P('row', 'col'), may hold values from -0.25 to 0.25
- slab: float32 [24576, 8192], P('row', 'col'), may hold values from -0.0390625 to 0.0390625
- slab_adj: float32 [24576, 8192], P('row', 'col'), may hold values from -6 to 6
- row_adj: float32 [512, 8192], P('row', 'col'), may hold values from -6 to 6
- diag_adj: float32 [512, 512], P('row', 'col'), may hold values from -6 to 6
Outputs:
- panel_out: float32 [24576, 512], P('row', 'col')
- slab_out: float32 [24576, 8192], P('row', 'col')
- row_out: float32 [512, 8192], P('row', 'col')
- diag_out: float32 [512, 512], P('row', 'col')
The draws below stay inside these ranges and needn't reach their ends.
Inputs may be any that keep to these rules, and one draw needn't show every extreme that they name: inv_tile is lower triangular with diagonal entries between 1 and 2.
All inputs are finite; a program needn't handle non-finite values.
Results may differ from the reference program's by a relative error of at most 0.00011.
Values sent between devices are 32-bit elements; how exact they have to be, the bound alone decides.
No kernel may reach another device: no remote copies, remote signals or barrier semaphores. Data moves between devices by JAX's collectives and lax.ppermute only.
A program may use at most 64 MiB of HBM per device.

```python
import math
import jax
import jax.numpy as jnp
from jax import lax

NB = 512
K = 8192
ROWS = 24576


def draw_inv_tile(key, part):
    first_key, second_key = jax.random.split(key)
    row_ids = lax.broadcasted_iota(jnp.int32, (NB, NB), 0)
    col_ids = lax.broadcasted_iota(jnp.int32, (NB, NB), 1)
    lower_part = jnp.clip(jax.random.normal(first_key, (NB, NB), jnp.float32) * (0.8 / math.sqrt(NB)), -0.95, 0.95)
    diagonal = jax.random.uniform(second_key, (NB, NB), jnp.float32, 1.0, 2.0)
    return jnp.where(row_ids > col_ids, lower_part, jnp.where(row_ids == col_ids, diagonal, 0.0))


def raised(array, rng, source, target, shards_of, factor):
    def block_of(position):
        return (jnp.arange(array.shape[position]) // (array.shape[position] // shards_of)).reshape((-1,) + (1,) * (array.ndim - 1 - position))

    one_side = jax.random.permutation(rng, shards_of)[block_of(target)]
    other_side = (block_of(target) + shards_of // 2) % shards_of
    return jnp.where((block_of(source) == one_side) | (block_of(source) == other_side), factor * array, array)


def block_scale(key, dims, cuts, smallest, largest):
    def one(position, blocks):
        heights = jax.random.uniform(jax.random.fold_in(jax.random.fold_in(key, 6), position), (blocks,), jnp.float32, smallest / len(cuts), largest / len(cuts))
        return jnp.repeat(jnp.exp(heights), dims[position] // blocks).reshape((-1,) + (1,) * (len(dims) - position - 1))

    level = one(*cuts[0])
    for cut in cuts[1:]:
        level = level * one(*cut)
    return level


def gaussian(rng, shape, spread, bound, shards=(), kind=jnp.bfloat16):
    entries = jax.random.normal(rng, shape, jnp.float32) * spread
    if len(shards) > 0:
        entries = block_scale(rng, shape, shards, -0.22, 0.18) * entries
    return jnp.clip(entries, min=-bound, max=bound).astype(kind)


def bell_draw_with(own_key, shape, scale, reach, cuts, heavy, kind=jnp.bfloat16):
    values = scale * jax.random.normal(own_key, shape, jnp.float32)
    if cuts:
        values = values * block_scale(own_key, shape, cuts, -0.22, 0.18)
    return jnp.clip(raised(values, jax.random.fold_in(own_key, 3), *heavy), -reach, reach).astype(kind)


def setup_inputs(seed: int = 0) -> dict:
    splits = jax.random.split(jax.random.key(seed), 9)
    panel_adj = bell_draw_with(splits[0], (ROWS, NB), 1.0, 16.0, ((0, 64), (1, 4)), (0, 1, 64, 4.0), jnp.float32)
    inv_tile = draw_inv_tile(jax.random.fold_in(splits[8], 71), 0)
    factor_panel = gaussian(splits[2], (ROWS, NB), ROWS ** -0.5, 0.0390625, ((0, 64), (1, 4)), jnp.float32)
    block_row = gaussian(splits[3], (NB, K), NB ** -0.5, 0.25, ((0, 64), (1, 4)), jnp.float32)
    slab = gaussian(splits[4], (ROWS, K), ROWS ** -0.5, 0.0390625, ((0, 64), (1, 4)), jnp.float32)
    slab_adj = gaussian(splits[5], (ROWS, K), 1.0, 6.0, ((0, 64), (1, 4)), jnp.float32)
    row_adj = gaussian(splits[6], (NB, K), 1.0, 6.0, ((0, 64), (1, 4)), jnp.float32)
    diag_adj = gaussian(splits[7], (NB, NB), 1.0, 6.0, ((0, 64), (1, 4)), jnp.float32)
    return dict(panel_adj=panel_adj, inv_tile=inv_tile, factor_panel=factor_panel, block_row=block_row, slab=slab, slab_adj=slab_adj, row_adj=row_adj, diag_adj=diag_adj)


def reference(panel_adj, inv_tile, factor_panel, block_row, slab, slab_adj, row_adj, diag_adj):
    precise = lax.Precision.HIGHEST
    scaled = jnp.dot(panel_adj, inv_tile, precision=precise, preferred_element_type=jnp.float32)
    slab_out = slab_adj - jnp.dot(scaled, block_row, precision=precise, preferred_element_type=jnp.float32)
    row_term = lax.dot_general(scaled, slab, (((0,), (0,)), ((), ())), precision=precise, preferred_element_type=jnp.float32)
    diag_term = lax.dot_general(scaled, factor_panel, (((0,), (0,)), ((), ())), precision=precise, preferred_element_type=jnp.float32)
    return scaled, slab_out, row_adj - row_term, diag_adj - jnp.tril(diag_term)
```

```python
import jax
import jax.numpy as jnp
from jax import lax
from jax.sharding import PartitionSpec as P


def contract_rows(left, right):
    return lax.dot_general(
        left,
        right,
        (((0,), (0,)), ((), ())),
        precision=lax.Precision.HIGHEST,
        preferred_element_type=jnp.float32,
    )


def bit_orders(bits):
    if bits == 6:
        return (0, 1, 3, 2, 4, 5), (0, 3, 1, 4, 2, 5)
    order = tuple(range(bits))
    return order, order


def swap_with(value, axis, size, bit):
    return lax.ppermute(value, axis, [(i, i ^ (1 << bit)) for i in range(size)])


def reduce_scatter_rows(stack, axis, size, order):
    bits = size.bit_length() - 1
    place = lax.axis_index(axis)
    tail = stack.shape[1:]
    held = stack.reshape((2,) * bits + tail)
    for bit in order:
        dim = bits - 1 - bit
        mine = (place >> bit) & 1
        low = lax.index_in_dim(held, 0, dim, keepdims=False)
        high = lax.index_in_dim(held, 1, dim, keepdims=False)
        keep = jnp.where(mine == 0, low, high)
        send = jnp.where(mine == 0, high, low)
        held = jnp.expand_dims(keep + swap_with(send, axis, size, bit), dim)
    return held.reshape(tail)


def all_gather_rows(piece, axis, size, order):
    bits = size.bit_length() - 1
    place = lax.axis_index(axis)
    tail = piece.shape
    held = piece.reshape((1,) * bits + tail)
    for bit in order:
        dim = bits - 1 - bit
        mine = (place >> bit) & 1
        other = swap_with(held, axis, size, bit)
        held = jnp.where(
            mine == 0,
            jnp.concatenate([held, other], dim),
            jnp.concatenate([other, held], dim),
        )
    return held.reshape((size * tail[0],) + tail[1:])


def per_device(panel_adj, inv_tile, factor_panel, block_row, slab, slab_adj, row_adj, diag_adj):
    precise = lax.Precision.HIGHEST
    rows_n = lax.axis_size("row")
    cols_n = lax.axis_size("col")
    col_width = panel_adj.shape[1]
    col_place = lax.axis_index("col")
    row_place = lax.axis_index("row")
    share = diag_adj.shape[0]
    first, second = bit_orders(rows_n.bit_length() - 1)

    half_k = block_row.shape[1] // 2
    gathered = jnp.concatenate(
        [
            all_gather_rows(block_row[:, :half_k], "row", rows_n, first[::-1]),
            all_gather_rows(block_row[:, half_k:], "row", rows_n, second[::-1]),
        ],
        axis=1,
    )

    partial_panel = jnp.dot(
        panel_adj, inv_tile, precision=precise, preferred_element_type=jnp.float32
    )
    parts = partial_panel.reshape(partial_panel.shape[0], cols_n, col_width)
    own = lax.dynamic_index_in_dim(parts, col_place, 1, keepdims=False)
    for shift in range(1, cols_n):
        target = jnp.maximum(col_place - shift, 0)
        piece = lax.dynamic_index_in_dim(parts, target, 1, keepdims=False)
        own = own + lax.ppermute(piece, "col", [(c, c - shift) for c in range(shift, cols_n)])
    panel_out = own
    blocks = [None] * cols_n
    for shift in range(cols_n):
        if shift == 0:
            got = own
        else:
            got = lax.ppermute(own, "col", [(c, (c + shift) % cols_n) for c in range(cols_n)])
        blocks[shift] = got
    stacked = jnp.stack(blocks, axis=0)
    scaled_blocks = [
        lax.dynamic_index_in_dim(stacked, (col_place - j) % cols_n, 0, keepdims=False)
        for j in range(cols_n)
    ]
    scaled = jnp.concatenate(scaled_blocks, axis=1)

    slab_out = slab_adj - jnp.dot(
        scaled, gathered, precision=precise, preferred_element_type=jnp.float32
    )
    row_term = contract_rows(scaled, slab)
    diag_term = contract_rows(scaled, factor_panel)
    width = row_term.shape[1]
    half_w = width // 2
    stack_a = jnp.concatenate([row_term[:, :half_w], diag_term], axis=1)
    stack_b = row_term[:, half_w:]
    sum_a = reduce_scatter_rows(stack_a.reshape(rows_n, share, -1), "row", rows_n, first)
    sum_b = reduce_scatter_rows(stack_b.reshape(rows_n, share, -1), "row", rows_n, second)
    row_sum = jnp.concatenate([sum_a[:, :half_w], sum_b], axis=1)
    diag_sum = sum_a[:, half_w:]

    row_ids = lax.broadcasted_iota(jnp.int32, diag_adj.shape, 0) + row_place * share
    col_ids = lax.broadcasted_iota(jnp.int32, diag_adj.shape, 1) + col_place * col_width
    diag_out = diag_adj - jnp.where(col_ids <= row_ids, diag_sum, 0.0)
    return (panel_out, slab_out, row_adj - row_sum, diag_out)


def solution(mesh):
    return jax.shard_map(
        per_device,
        mesh=mesh,
        in_specs=(
            P("row", "col"),
            P("col", None),
            P("row", "col"),
            P("row", "col"),
            P("row", "col"),
            P("row", "col"),
            P("row", "col"),
            P("row", "col"),
        ),
        out_specs=(P("row", "col"), P("row", "col"), P("row", "col"), P("row", "col")),
        check_vma=False,
    )
```

```python
import jax
import jax.numpy as jnp
from jax import lax
from jax.sharding import PartitionSpec as P


def contract_rows(left, right, precision=lax.Precision.HIGHEST):
    return lax.dot_general(
        left,
        right,
        (((0,), (0,)), ((), ())),
        precision=precision,
        preferred_element_type=jnp.float32,
    )


def bit_orders(bits):
    if bits == 6:
        return (0, 1, 3, 2, 4, 5), (0, 3, 1, 4, 2, 5)
    order = tuple(range(bits))
    return order, order


def swap_with(value, axis, size, bit):
    return lax.ppermute(value, axis, [(i, i ^ (1 << bit)) for i in range(size)])


def reduce_scatter_rows(stack, axis, size, order):
    bits = size.bit_length() - 1
    place = lax.axis_index(axis)
    tail = stack.shape[1:]
    held = stack.reshape((2,) * bits + tail)
    for bit in order:
        dim = bits - 1 - bit
        mine = (place >> bit) & 1
        low = lax.index_in_dim(held, 0, dim, keepdims=False)
        high = lax.index_in_dim(held, 1, dim, keepdims=False)
        keep = jnp.where(mine == 0, low, high)
        send = jnp.where(mine == 0, high, low)
        held = jnp.expand_dims(keep + swap_with(send, axis, size, bit), dim)
    return held.reshape(tail)


def all_gather_rows(piece, axis, size, order):
    bits = size.bit_length() - 1
    place = lax.axis_index(axis)
    tail = piece.shape
    held = piece.reshape((1,) * bits + tail)
    for bit in order:
        dim = bits - 1 - bit
        mine = (place >> bit) & 1
        other = swap_with(held, axis, size, bit)
        held = jnp.where(
            mine == 0,
            jnp.concatenate([held, other], dim),
            jnp.concatenate([other, held], dim),
        )
    return held.reshape((size * tail[0],) + tail[1:])


def per_device(panel_adj, inv_tile, factor_panel, block_row, slab, slab_adj, row_adj, diag_adj):
    precise = lax.Precision.HIGHEST
    rows_n = lax.axis_size("row")
    cols_n = lax.axis_size("col")
    col_width = panel_adj.shape[1]
    col_place = lax.axis_index("col")
    row_place = lax.axis_index("row")
    share = diag_adj.shape[0]
    first, second = bit_orders(rows_n.bit_length() - 1)

    gathered = lax.all_gather(block_row, "row", axis=0, tiled=True)

    partial_panel = jnp.dot(
        panel_adj, inv_tile, precision=precise, preferred_element_type=jnp.float32
    )
    parts = partial_panel.reshape(partial_panel.shape[0], cols_n, col_width)
    own = lax.dynamic_index_in_dim(parts, col_place, 1, keepdims=False)
    for shift in range(1, cols_n):
        target = jnp.maximum(col_place - shift, 0)
        piece = lax.dynamic_index_in_dim(parts, target, 1, keepdims=False)
        own = own + lax.ppermute(piece, "col", [(c, c - shift) for c in range(shift, cols_n)])
    panel_out = own
    blocks = [None] * cols_n
    for shift in range(cols_n):
        if shift == 0:
            got = own
        else:
            got = lax.ppermute(own, "col", [(c, (c + shift) % cols_n) for c in range(cols_n)])
        blocks[shift] = got
    stacked = jnp.stack(blocks, axis=0)
    scaled_blocks = [
        lax.dynamic_index_in_dim(stacked, (col_place - j) % cols_n, 0, keepdims=False)
        for j in range(cols_n)
    ]
    scaled = jnp.concatenate(scaled_blocks, axis=1)

    slab_out = slab_adj - jnp.dot(
        scaled, gathered, precision=lax.Precision.HIGH, preferred_element_type=jnp.float32
    )
    row_term = contract_rows(scaled, slab, lax.Precision.HIGH)
    diag_term = contract_rows(scaled, factor_panel)
    width = row_term.shape[1]
    half_w = width // 2
    stack_a = jnp.concatenate([row_term[:, :half_w], diag_term], axis=1)
    stack_b = row_term[:, half_w:]
    sum_a = reduce_scatter_rows(stack_a.reshape(rows_n, share, -1), "row", rows_n, first)
    sum_b = reduce_scatter_rows(stack_b.reshape(rows_n, share, -1), "row", rows_n, second)
    row_sum = jnp.concatenate([sum_a[:, :half_w], sum_b], axis=1)
    diag_sum = sum_a[:, half_w:]

    row_ids = lax.broadcasted_iota(jnp.int32, diag_adj.shape, 0) + row_place * share
    col_ids = lax.broadcasted_iota(jnp.int32, diag_adj.shape, 1) + col_place * col_width
    diag_out = diag_adj - jnp.where(col_ids <= row_ids, diag_sum, 0.0)
    return (panel_out, slab_out, row_adj - row_sum, diag_out)


def solution(mesh):
    return jax.shard_map(
        per_device,
        mesh=mesh,
        in_specs=(
            P("row", "col"),
            P("col", None),
            P("row", "col"),
            P("row", "col"),
            P("row", "col"),
            P("row", "col"),
            P("row", "col"),
            P("row", "col"),
        ),
        out_specs=(P("row", "col"), P("row", "col"), P("row", "col"), P("row", "col")),
        check_vma=False,
    )
```

```python
import jax
import jax.numpy as jnp
from jax import lax
from jax.sharding import PartitionSpec as P


def contract_rows(left, right, precision=lax.Precision.HIGHEST):
    return lax.dot_general(
        left,
        right,
        (((0,), (0,)), ((), ())),
        precision=precision,
        preferred_element_type=jnp.float32,
    )


def bit_orders(bits):
    if bits == 6:
        return (0, 1, 3, 2, 4, 5), (0, 3, 1, 4, 2, 5)
    order = tuple(range(bits))
    return order, order


def swap_with(value, axis, size, bit):
    return lax.ppermute(value, axis, [(i, i ^ (1 << bit)) for i in range(size)])


def reduce_scatter_rows(stack, axis, size, order):
    bits = size.bit_length() - 1
    place = lax.axis_index(axis)
    tail = stack.shape[1:]
    held = stack.reshape((2,) * bits + tail)
    for bit in order:
        dim = bits - 1 - bit
        mine = (place >> bit) & 1
        low = lax.index_in_dim(held, 0, dim, keepdims=False)
        high = lax.index_in_dim(held, 1, dim, keepdims=False)
        keep = jnp.where(mine == 0, low, high)
        send = jnp.where(mine == 0, high, low)
        held = jnp.expand_dims(keep + swap_with(send, axis, size, bit), dim)
    return held.reshape(tail)


def all_gather_rows(piece, axis, size, order):
    bits = size.bit_length() - 1
    place = lax.axis_index(axis)
    tail = piece.shape
    held = piece.reshape((1,) * bits + tail)
    for bit in order:
        dim = bits - 1 - bit
        mine = (place >> bit) & 1
        other = swap_with(held, axis, size, bit)
        held = jnp.where(
            mine == 0,
            jnp.concatenate([held, other], dim),
            jnp.concatenate([other, held], dim),
        )
    return held.reshape((size * tail[0],) + tail[1:])


def per_device(panel_adj, inv_tile, factor_panel, block_row, slab, slab_adj, row_adj, diag_adj):
    precise = lax.Precision.HIGHEST
    rows_n = lax.axis_size("row")
    cols_n = lax.axis_size("col")
    col_width = panel_adj.shape[1]
    col_place = lax.axis_index("col")
    row_place = lax.axis_index("row")
    share = diag_adj.shape[0]
    first, second = bit_orders(rows_n.bit_length() - 1)

    gathered = lax.all_gather(block_row, "row", axis=0, tiled=True)

    def times_inv_columns(block):
        columns = lax.dynamic_slice_in_dim(inv_tile, block * col_width, col_width, 1)
        return jnp.dot(panel_adj, columns, precision=precise, preferred_element_type=jnp.float32)

    own = times_inv_columns(col_place)
    for shift in range(1, cols_n):
        piece = times_inv_columns(jnp.maximum(col_place - shift, 0))
        own = own + lax.ppermute(piece, "col", [(c, c - shift) for c in range(shift, cols_n)])
    panel_out = own
    blocks = [None] * cols_n
    for shift in range(cols_n):
        if shift == 0:
            got = own
        else:
            got = lax.ppermute(own, "col", [(c, (c + shift) % cols_n) for c in range(cols_n)])
        blocks[shift] = got
    stacked = jnp.stack(blocks, axis=0)
    scaled_blocks = [
        lax.dynamic_index_in_dim(stacked, (col_place - j) % cols_n, 0, keepdims=False)
        for j in range(cols_n)
    ]
    scaled = jnp.concatenate(scaled_blocks, axis=1)

    slab_out = slab_adj - jnp.dot(
        scaled, gathered, precision=lax.Precision.HIGH, preferred_element_type=jnp.float32
    )
    row_term = contract_rows(scaled, slab, lax.Precision.HIGH)
    diag_term = contract_rows(scaled, factor_panel)
    width = row_term.shape[1]
    half_w = width // 2
    stack_a = jnp.concatenate([row_term[:, :half_w], diag_term], axis=1)
    stack_b = row_term[:, half_w:]
    sum_a = reduce_scatter_rows(stack_a.reshape(rows_n, share, -1), "row", rows_n, first)
    sum_b = reduce_scatter_rows(stack_b.reshape(rows_n, share, -1), "row", rows_n, second)
    row_sum = jnp.concatenate([sum_a[:, :half_w], sum_b], axis=1)
    diag_sum = sum_a[:, half_w:]

    row_ids = lax.broadcasted_iota(jnp.int32, diag_adj.shape, 0) + row_place * share
    col_ids = lax.broadcasted_iota(jnp.int32, diag_adj.shape, 1) + col_place * col_width
    diag_out = diag_adj - jnp.where(col_ids <= row_ids, diag_sum, 0.0)
    return (panel_out, slab_out, row_adj - row_sum, diag_out)


def solution(mesh):
    return jax.shard_map(
        per_device,
        mesh=mesh,
        in_specs=(
            P("row", "col"),
            P("col", None),
            P("row", "col"),
            P("row", "col"),
            P("row", "col"),
            P("row", "col"),
            P("row", "col"),
            P("row", "col"),
        ),
        out_specs=(P("row", "col"), P("row", "col"), P("row", "col"), P("row", "col")),
        check_vma=False,
    )
```

```python
import jax
import jax.numpy as jnp
from jax import lax
from jax.sharding import PartitionSpec as P


def contract_rows(left, right, precision=lax.Precision.HIGHEST):
    return lax.dot_general(
        left,
        right,
        (((0,), (0,)), ((), ())),
        precision=precision,
        preferred_element_type=jnp.float32,
    )


def bit_orders(bits):
    if bits == 6:
        return (0, 1, 3, 2, 4, 5), (0, 3, 1, 4, 2, 5)
    order = tuple(range(bits))
    return order, order


def swap_with(value, axis, size, bit):
    return lax.ppermute(value, axis, [(i, i ^ (1 << bit)) for i in range(size)])


def halve(held, axis, size, bit):
    bits = size.bit_length() - 1
    dim = bits - 1 - bit
    mine = (lax.axis_index(axis) >> bit) & 1
    low = lax.index_in_dim(held, 0, dim, keepdims=False)
    high = lax.index_in_dim(held, 1, dim, keepdims=False)
    keep = jnp.where(mine == 0, low, high)
    send = jnp.where(mine == 0, high, low)
    return jnp.expand_dims(keep + swap_with(send, axis, size, bit), dim)


def reduce_scatter_rows(stack, axis, size, split):
    bits = size.bit_length() - 1
    tail = stack.shape[1:]
    held = stack.reshape((2,) * bits + tail)
    if bits == 6:
        held = halve(held, axis, size, 0)
        part_a, part_b = held[..., :split], held[..., split:]
        for bit in (1, 3):
            part_a = halve(part_a, axis, size, bit)
        for bit in (3, 1):
            part_b = halve(part_b, axis, size, bit)
        held = jnp.concatenate([part_a, part_b], axis=-1)
        order = (2, 4, 5)
    else:
        order = tuple(range(bits))
    for bit in order:
        held = halve(held, axis, size, bit)
    return held.reshape(tail)


def all_gather_rows(piece, axis, size, order):
    bits = size.bit_length() - 1
    place = lax.axis_index(axis)
    tail = piece.shape
    held = piece.reshape((1,) * bits + tail)
    for bit in order:
        dim = bits - 1 - bit
        mine = (place >> bit) & 1
        other = swap_with(held, axis, size, bit)
        held = jnp.where(
            mine == 0,
            jnp.concatenate([held, other], dim),
            jnp.concatenate([other, held], dim),
        )
    return held.reshape((size * tail[0],) + tail[1:])


def per_device(panel_adj, inv_tile, factor_panel, block_row, slab, slab_adj, row_adj, diag_adj):
    precise = lax.Precision.HIGHEST
    rows_n = lax.axis_size("row")
    cols_n = lax.axis_size("col")
    col_width = panel_adj.shape[1]
    col_place = lax.axis_index("col")
    row_place = lax.axis_index("row")
    share = diag_adj.shape[0]
    first, second = bit_orders(rows_n.bit_length() - 1)

    gathered = lax.all_gather(block_row, "row", axis=0, tiled=True)

    def times_inv_columns(block):
        columns = lax.dynamic_slice_in_dim(inv_tile, block * col_width, col_width, 1)
        return jnp.dot(panel_adj, columns, precision=precise, preferred_element_type=jnp.float32)

    own = times_inv_columns(col_place)
    for shift in range(1, cols_n):
        piece = times_inv_columns(jnp.maximum(col_place - shift, 0))
        own = own + lax.ppermute(piece, "col", [(c, c - shift) for c in range(shift, cols_n)])
    panel_out = own
    blocks = [None] * cols_n
    for shift in range(cols_n):
        if shift == 0:
            got = own
        else:
            got = lax.ppermute(own, "col", [(c, (c + shift) % cols_n) for c in range(cols_n)])
        blocks[shift] = got
    stacked = jnp.stack(blocks, axis=0)
    scaled_blocks = [
        lax.dynamic_index_in_dim(stacked, (col_place - j) % cols_n, 0, keepdims=False)
        for j in range(cols_n)
    ]
    scaled = jnp.concatenate(scaled_blocks, axis=1)

    slab_out = slab_adj - jnp.dot(
        scaled, gathered, precision=lax.Precision.HIGH, preferred_element_type=jnp.float32
    )
    row_term = contract_rows(scaled, slab, lax.Precision.HIGH)
    diag_term = contract_rows(scaled, factor_panel)
    width = row_term.shape[1]
    stack = jnp.concatenate([row_term, diag_term], axis=1)
    summed = reduce_scatter_rows(stack.reshape(rows_n, share, -1), "row", rows_n, width // 2 + 128)
    row_sum = summed[:, :width]
    diag_sum = summed[:, width:]

    row_ids = lax.broadcasted_iota(jnp.int32, diag_adj.shape, 0) + row_place * share
    col_ids = lax.broadcasted_iota(jnp.int32, diag_adj.shape, 1) + col_place * col_width
    diag_out = diag_adj - jnp.where(col_ids <= row_ids, diag_sum, 0.0)
    return (panel_out, slab_out, row_adj - row_sum, diag_out)


def solution(mesh):
    return jax.shard_map(
        per_device,
        mesh=mesh,
        in_specs=(
            P("row", "col"),
            P("col", None),
            P("row", "col"),
            P("row", "col"),
            P("row", "col"),
            P("row", "col"),
            P("row", "col"),
            P("row", "col"),
        ),
        out_specs=(P("row", "col"), P("row", "col"), P("row", "col"), P("row", "col")),
        check_vma=False,
    )
```

```python
import jax
import jax.numpy as jnp
from jax import lax
from jax.sharding import Mesh, PartitionSpec as P

ROW = ("rz", "core")


def contract_rows(left, right, precision=lax.Precision.HIGHEST):
    return lax.dot_general(
        left,
        right,
        (((0,), (0,)), ((), ())),
        precision=precision,
        preferred_element_type=jnp.float32,
    )


def bit_orders(bits):
    if bits == 6:
        return (0, 1, 3, 2, 4, 5), (0, 3, 1, 4, 2, 5)
    order = tuple(range(bits))
    return order, order


def swap_with(value, axis, size, bit):
    return lax.ppermute(value, axis, [(i, i ^ (1 << bit)) for i in range(size)])


def halve(held, axis, size, bit):
    bits = size.bit_length() - 1
    dim = bits - 1 - bit
    mine = (lax.axis_index(axis) >> bit) & 1
    low = lax.index_in_dim(held, 0, dim, keepdims=False)
    high = lax.index_in_dim(held, 1, dim, keepdims=False)
    keep = jnp.where(mine == 0, low, high)
    send = jnp.where(mine == 0, high, low)
    return jnp.expand_dims(keep + swap_with(send, axis, size, bit), dim)


def reduce_scatter_rows(stack, axis, size, split):
    bits = size.bit_length() - 1
    tail = stack.shape[1:]
    held = stack.reshape((2,) * bits + tail)
    if bits == 6:
        held = halve(held, axis, size, 0)
        part_a, part_b = held[..., :split], held[..., split:]
        for bit in (1, 3):
            part_a = halve(part_a, axis, size, bit)
        for bit in (3, 1):
            part_b = halve(part_b, axis, size, bit)
        held = jnp.concatenate([part_a, part_b], axis=-1)
        order = (2, 4, 5)
    else:
        order = tuple(range(bits))
    for bit in order:
        held = halve(held, axis, size, bit)
    return held.reshape(tail)


def all_gather_rows(piece, axis, size, order):
    bits = size.bit_length() - 1
    place = lax.axis_index(axis)
    tail = piece.shape
    held = piece.reshape((1,) * bits + tail)
    for bit in order:
        dim = bits - 1 - bit
        mine = (place >> bit) & 1
        other = swap_with(held, axis, size, bit)
        held = jnp.where(
            mine == 0,
            jnp.concatenate([held, other], dim),
            jnp.concatenate([other, held], dim),
        )
    return held.reshape((size * tail[0],) + tail[1:])


def per_device(panel_adj, inv_tile, factor_panel, block_row, slab, slab_adj, row_adj, diag_adj):
    precise = lax.Precision.HIGHEST
    rows_n = lax.axis_size("rz") * lax.axis_size("core")
    cols_n = lax.axis_size("col")
    col_width = panel_adj.shape[1]
    col_place = lax.axis_index("col")
    row_place = lax.axis_index(ROW)
    share = diag_adj.shape[0]
    first, second = bit_orders(rows_n.bit_length() - 1)

    own_core = lax.all_gather(block_row, "rz", axis=0)
    other_core = lax.ppermute(own_core, "core", [(0, 1), (1, 0)])
    core = lax.axis_index("core")
    gathered = jnp.where(
        core == 0,
        jnp.stack([own_core, other_core], axis=1),
        jnp.stack([other_core, own_core], axis=1),
    ).reshape((rows_n * block_row.shape[0],) + block_row.shape[1:])

    def times_inv_columns(block):
        columns = lax.dynamic_slice_in_dim(inv_tile, block * col_width, col_width, 1)
        return jnp.dot(panel_adj, columns, precision=precise, preferred_element_type=jnp.float32)

    own = times_inv_columns(col_place)
    for shift in range(1, cols_n):
        piece = times_inv_columns(jnp.maximum(col_place - shift, 0))
        own = own + lax.ppermute(piece, "col", [(c, c - shift) for c in range(shift, cols_n)])
    panel_out = own
    blocks = [None] * cols_n
    for shift in range(cols_n):
        if shift == 0:
            got = own
        else:
            got = lax.ppermute(own, "col", [(c, (c + shift) % cols_n) for c in range(cols_n)])
        blocks[shift] = got
    stacked = jnp.stack(blocks, axis=0)
    scaled_blocks = [
        lax.dynamic_index_in_dim(stacked, (col_place - j) % cols_n, 0, keepdims=False)
        for j in range(cols_n)
    ]
    scaled = jnp.concatenate(scaled_blocks, axis=1)

    slab_out = slab_adj - jnp.dot(
        scaled, gathered, precision=lax.Precision.HIGH, preferred_element_type=jnp.float32
    )
    row_term = contract_rows(scaled, slab, lax.Precision.HIGH)
    diag_term = contract_rows(scaled, factor_panel)
    width = row_term.shape[1]
    stack = jnp.concatenate([row_term, diag_term], axis=1)
    summed = reduce_scatter_rows(stack.reshape(rows_n, share, -1), ROW, rows_n, width // 2 + 128)
    row_sum = summed[:, :width]
    diag_sum = summed[:, width:]

    row_ids = lax.broadcasted_iota(jnp.int32, diag_adj.shape, 0) + row_place * share
    col_ids = lax.broadcasted_iota(jnp.int32, diag_adj.shape, 1) + col_place * col_width
    diag_out = diag_adj - jnp.where(col_ids <= row_ids, diag_sum, 0.0)
    return (panel_out, slab_out, row_adj - row_sum, diag_out)


def solution(mesh):
    rows, cols = mesh.shape["row"], mesh.shape["col"]
    split = Mesh(mesh.devices.reshape(rows // 2, 2, cols), ("rz", "core", "col"))
    tiled = P(ROW, "col")
    return jax.shard_map(
        per_device,
        mesh=split,
        in_specs=(tiled, P("col", None), tiled, tiled, tiled, tiled, tiled, tiled),
        out_specs=(tiled, tiled, tiled, tiled),
        check_vma=False,
    )
```

```python
import jax
import jax.numpy as jnp
from jax import lax
from jax.sharding import PartitionSpec as P


def contract_rows(left, right, precision=lax.Precision.HIGHEST):
    return lax.dot_general(
        left,
        right,
        (((0,), (0,)), ((), ())),
        precision=precision,
        preferred_element_type=jnp.float32,
    )


def bit_orders(bits):
    if bits == 6:
        return (0, 1, 3, 2, 4, 5), (0, 3, 1, 4, 2, 5)
    order = tuple(range(bits))
    return order, order


def swap_with(value, axis, size, bit):
    return lax.ppermute(value, axis, [(i, i ^ (1 << bit)) for i in range(size)])


def halve(held, axis, size, bit):
    bits = size.bit_length() - 1
    dim = bits - 1 - bit
    mine = (lax.axis_index(axis) >> bit) & 1
    low = lax.index_in_dim(held, 0, dim, keepdims=False)
    high = lax.index_in_dim(held, 1, dim, keepdims=False)
    keep = jnp.where(mine == 0, low, high)
    send = jnp.where(mine == 0, high, low)
    return jnp.expand_dims(keep + swap_with(send, axis, size, bit), dim)


def reduce_scatter_rows(stack, axis, size, split):
    bits = size.bit_length() - 1
    tail = stack.shape[1:]
    held = stack.reshape((2,) * bits + tail)
    if bits == 6:
        held = halve(held, axis, size, 0)
        part_a, part_b = held[..., :split], held[..., split:]
        for bit in (1, 3):
            part_a = halve(part_a, axis, size, bit)
        for bit in (3, 1):
            part_b = halve(part_b, axis, size, bit)
        held = jnp.concatenate([part_a, part_b], axis=-1)
        order = (2, 4, 5)
    else:
        order = tuple(range(bits))
    for bit in order:
        held = halve(held, axis, size, bit)
    return held.reshape(tail)


def all_gather_rows(piece, axis, size, order):
    bits = size.bit_length() - 1
    place = lax.axis_index(axis)
    tail = piece.shape
    held = piece.reshape((1,) * bits + tail)
    for bit in order:
        dim = bits - 1 - bit
        mine = (place >> bit) & 1
        other = swap_with(held, axis, size, bit)
        held = jnp.where(
            mine == 0,
            jnp.concatenate([held, other], dim),
            jnp.concatenate([other, held], dim),
        )
    return held.reshape((size * tail[0],) + tail[1:])


def per_device(panel_adj, inv_tile, factor_panel, block_row, slab, slab_adj, row_adj, diag_adj):
    precise = lax.Precision.HIGHEST
    rows_n = lax.axis_size("row")
    cols_n = lax.axis_size("col")
    col_width = panel_adj.shape[1]
    col_place = lax.axis_index("col")
    row_place = lax.axis_index("row")
    share = diag_adj.shape[0]
    first, second = bit_orders(rows_n.bit_length() - 1)

    half_k = block_row.shape[1] // 2
    gathered = jnp.concatenate(
        [
            all_gather_rows(block_row[:, :half_k], "row", rows_n, first[::-1]),
            all_gather_rows(block_row[:, half_k:], "row", rows_n, second[::-1]),
        ],
        axis=1,
    )

    def times_inv_columns(block):
        columns = lax.dynamic_slice_in_dim(inv_tile, block * col_width, col_width, 1)
        return jnp.dot(panel_adj, columns, precision=precise, preferred_element_type=jnp.float32)

    own = times_inv_columns(col_place)
    for shift in range(1, cols_n):
        piece = times_inv_columns(jnp.maximum(col_place - shift, 0))
        own = own + lax.ppermute(piece, "col", [(c, c - shift) for c in range(shift, cols_n)])
    panel_out = own
    blocks = [None] * cols_n
    for shift in range(cols_n):
        if shift == 0:
            got = own
        else:
            got = lax.ppermute(own, "col", [(c, (c + shift) % cols_n) for c in range(cols_n)])
        blocks[shift] = got
    stacked = jnp.stack(blocks, axis=0)
    scaled_blocks = [
        lax.dynamic_index_in_dim(stacked, (col_place - j) % cols_n, 0, keepdims=False)
        for j in range(cols_n)
    ]
    scaled = jnp.concatenate(scaled_blocks, axis=1)

    slab_out = slab_adj - jnp.dot(
        scaled, gathered, precision=lax.Precision.HIGH, preferred_element_type=jnp.float32
    )
    row_term = contract_rows(scaled, slab, lax.Precision.HIGH)
    diag_term = contract_rows(scaled, factor_panel)
    width = row_term.shape[1]
    stack = jnp.concatenate([row_term, diag_term], axis=1)
    summed = reduce_scatter_rows(stack.reshape(rows_n, share, -1), "row", rows_n, width // 2 + 128)
    row_sum = summed[:, :width]
    diag_sum = summed[:, width:]

    row_ids = lax.broadcasted_iota(jnp.int32, diag_adj.shape, 0) + row_place * share
    col_ids = lax.broadcasted_iota(jnp.int32, diag_adj.shape, 1) + col_place * col_width
    diag_out = diag_adj - jnp.where(col_ids <= row_ids, diag_sum, 0.0)
    return (panel_out, slab_out, row_adj - row_sum, diag_out)


def solution(mesh):
    return jax.shard_map(
        per_device,
        mesh=mesh,
        in_specs=(
            P("row", "col"),
            P("col", None),
            P("row", "col"),
            P("row", "col"),
            P("row", "col"),
            P("row", "col"),
            P("row", "col"),
            P("row", "col"),
        ),
        out_specs=(P("row", "col"), P("row", "col"), P("row", "col"), P("row", "col")),
        check_vma=False,
    )
```

```python
import jax
import jax.numpy as jnp
from jax import lax
from jax.sharding import PartitionSpec as P


def contract_rows(left, right):
    return lax.dot_general(
        left,
        right,
        (((0,), (0,)), ((), ())),
        precision=lax.Precision.HIGHEST,
        preferred_element_type=jnp.float32,
    )


def bit_orders(bits):
    if bits == 6:
        return (0, 1, 3, 2, 4, 5), (0, 3, 1, 4, 2, 5)
    order = tuple(range(bits))
    return order, order


def swap_with(value, axis, size, bit):
    return lax.ppermute(value, axis, [(i, i ^ (1 << bit)) for i in range(size)])


def reduce_scatter_rows(stack, axis, size, order):
    bits = size.bit_length() - 1
    place = lax.axis_index(axis)
    tail = stack.shape[1:]
    held = stack.reshape((2,) * bits + tail)
    for bit in order:
        dim = bits - 1 - bit
        mine = (place >> bit) & 1
        low = lax.index_in_dim(held, 0, dim, keepdims=False)
        high = lax.index_in_dim(held, 1, dim, keepdims=False)
        keep = jnp.where(mine == 0, low, high)
        send = jnp.where(mine == 0, high, low)
        held = jnp.expand_dims(keep + swap_with(send, axis, size, bit), dim)
    return held.reshape(tail)


def all_gather_rows(piece, axis, size, order):
    bits = size.bit_length() - 1
    place = lax.axis_index(axis)
    tail = piece.shape
    held = piece.reshape((1,) * bits + tail)
    for bit in order:
        dim = bits - 1 - bit
        mine = (place >> bit) & 1
        other = swap_with(held, axis, size, bit)
        held = jnp.where(
            mine == 0,
            jnp.concatenate([held, other], dim),
            jnp.concatenate([other, held], dim),
        )
    return held.reshape((size * tail[0],) + tail[1:])


def per_device(panel_adj, inv_tile, factor_panel, block_row, slab, slab_adj, row_adj, diag_adj):
    precise = lax.Precision.HIGHEST
    rows_n = lax.axis_size("row")
    cols_n = lax.axis_size("col")
    col_width = panel_adj.shape[1]
    col_place = lax.axis_index("col")
    row_place = lax.axis_index("row")
    share = diag_adj.shape[0]
    first, second = bit_orders(rows_n.bit_length() - 1)

    half_k = block_row.shape[1] // 2
    gathered = jnp.concatenate(
        [
            all_gather_rows(block_row[:, :half_k], "row", rows_n, first[::-1]),
            all_gather_rows(block_row[:, half_k:], "row", rows_n, second[::-1]),
        ],
        axis=1,
    )

    def times_inv_columns(block):
        columns = lax.dynamic_slice_in_dim(inv_tile, block * col_width, col_width, 1)
        return jnp.dot(panel_adj, columns, precision=precise, preferred_element_type=jnp.float32)

    own = times_inv_columns(col_place)
    for shift in range(1, cols_n):
        piece = times_inv_columns(jnp.maximum(col_place - shift, 0))
        own = own + lax.ppermute(piece, "col", [(c, c - shift) for c in range(shift, cols_n)])
    panel_out = own
    blocks = [None] * cols_n
    for shift in range(cols_n):
        if shift == 0:
            got = own
        else:
            got = lax.ppermute(own, "col", [(c, (c + shift) % cols_n) for c in range(cols_n)])
        blocks[shift] = got
    stacked = jnp.stack(blocks, axis=0)
    scaled_blocks = [
        lax.dynamic_index_in_dim(stacked, (col_place - j) % cols_n, 0, keepdims=False)
        for j in range(cols_n)
    ]
    scaled = jnp.concatenate(scaled_blocks, axis=1)

    slab_out = slab_adj - jnp.dot(
        scaled, gathered, precision=precise, preferred_element_type=jnp.float32
    )
    row_term = contract_rows(scaled, slab)
    diag_term = contract_rows(scaled, factor_panel)
    width = row_term.shape[1]
    half_w = width // 2
    stack_a = jnp.concatenate([row_term[:, :half_w], diag_term], axis=1)
    stack_b = row_term[:, half_w:]
    sum_a = reduce_scatter_rows(stack_a.reshape(rows_n, share, -1), "row", rows_n, first)
    sum_b = reduce_scatter_rows(stack_b.reshape(rows_n, share, -1), "row", rows_n, second)
    row_sum = jnp.concatenate([sum_a[:, :half_w], sum_b], axis=1)
    diag_sum = sum_a[:, half_w:]

    row_ids = lax.broadcasted_iota(jnp.int32, diag_adj.shape, 0) + row_place * share
    col_ids = lax.broadcasted_iota(jnp.int32, diag_adj.shape, 1) + col_place * col_width
    diag_out = diag_adj - jnp.where(col_ids <= row_ids, diag_sum, 0.0)
    return (panel_out, slab_out, row_adj - row_sum, diag_out)


def solution(mesh):
    return jax.shard_map(
        per_device,
        mesh=mesh,
        in_specs=(
            P("row", "col"),
            P("col", None),
            P("row", "col"),
            P("row", "col"),
            P("row", "col"),
            P("row", "col"),
            P("row", "col"),
            P("row", "col"),
        ),
        out_specs=(P("row", "col"), P("row", "col"), P("row", "col"), P("row", "col")),
        check_vma=False,
    )
```
